512 devices in a mesh: dp: 8 (over y_hi, x), row: 16 (over z, core), col: 4 (over y_lo).
Axes of the slice: x: 4, y: 8 (y_hi: 2, y_lo: 4; y = y_hi * 4 + y_lo), z: 8, core: 2. Of those that a mesh axis runs over, the one named last changes fastest.
Arguments:
- layer_input: bfloat16 [16384, 8192], P(('dp', 'row'), 'col'), may hold values from -6 to 6
- gate_pre: bfloat16 [16384, 6656], P(('dp', 'col'), 'row'), may hold values from -10 to 10
- up_value: bfloat16 [16384, 6656], P(('dp', 'col'), 'row'), may hold values from -6 to 6
- grad_hidden: bfloat16 [16384, 6656], P(('dp', 'col'), 'row'), may hold values from -0.046875 to 0.046875
Outputs:
- gate_weight_grad: bfloat16 [6656, 4, 2048], P('row', 'col', 'dp')
- up_weight_grad: bfloat16 [6656, 4, 2048], P('row', 'col', 'dp')
The draws below stay inside these ranges and needn't reach their ends.
All inputs are finite; a program needn't handle non-finite values.
Results may differ from the reference program's by a relative error of at most 0.014.
Values may be sent and summed in bfloat16 or wider, within the bound.
No kernel may reach another device: no remote copies, remote signals or barrier semaphores. Data moves between devices by JAX's collectives and lax.ppermute only.
A program may use at most 64 MiB of HBM per device.

```python
import jax
import jax.numpy as jnp
from jax import lax

D = 8192
FF = 6656
RTOK = 2048
TOKENS = 16384
N_DP = 8
N_COL = 4


def levels(key, dims, split, least, top_value):
    factor_of, own = 1.0, jax.random.fold_in(key, 6)
    for axis_at, shards_of in split:
        steps = jnp.exp(jax.random.uniform(jax.random.fold_in(own, axis_at), (shards_of,), jnp.float32, least / len(split), top_value / len(split)))
        factor_of = factor_of * jnp.repeat(steps, dims[axis_at] // shards_of).reshape([-1 if axis == axis_at else 1 for axis in range(len(dims))])
    return factor_of


def bell_draw(own_key, dims, deviation, most, cuts=(), kind=jnp.bfloat16):
    factor_of = levels(own_key, dims, cuts, -0.22, 0.18) if cuts else 1.0
    drawn = jax.random.normal(own_key, dims, jnp.float32) * deviation * factor_of
    return jnp.minimum(jnp.maximum(drawn, -most), most).astype(kind)


def setup_inputs(seed: int = 0) -> dict:
    arg_keys = jax.random.split(jax.random.key(seed), 5)
    return {
        "layer_input": bell_draw(arg_keys[0], (TOKENS, D), 1.0, 6.0, ((0, 128), (1, 4))),
        "gate_pre": bell_draw(arg_keys[1], (TOKENS, FF), 2.0, 10.0, ((0, 32), (1, 16))),
        "up_value": bell_draw(arg_keys[2], (TOKENS, FF), 1.0, 6.0, ((0, 32), (1, 16))),
        "grad_hidden": bell_draw(arg_keys[3], (TOKENS, FF), (TOKENS ** -0.5), 0.046875, ((0, 32), (1, 16))),
    }


def reference(layer_input, gate_pre, up_value, grad_hidden):
    gate32 = gate_pre.astype(jnp.float32)
    sig = 1.0 / (1.0 + jnp.exp(-gate32))
    hid32 = grad_hidden.astype(jnp.float32)
    grad_up = (hid32 * gate32 * sig).astype(jnp.bfloat16)
    grad_gate = (hid32 * up_value.astype(jnp.float32) * sig * (1.0 + gate32 * (1.0 - sig))).astype(jnp.bfloat16)
    gate_total = jnp.zeros((FF, D), jnp.float32)
    up_total = jnp.zeros((FF, D), jnp.float32)
    for replica in range(N_DP):
        lo = replica * RTOK
        inputs = layer_input[lo:lo + RTOK]
        gate_part = lax.dot_general(grad_gate[lo:lo + RTOK], inputs, (((0,), (0,)), ((), ())), preferred_element_type=jnp.float32)
        up_part = lax.dot_general(grad_up[lo:lo + RTOK], inputs, (((0,), (0,)), ((), ())), preferred_element_type=jnp.float32)
        gate_total = gate_total + gate_part.astype(jnp.bfloat16).astype(jnp.float32)
        up_total = up_total + up_part.astype(jnp.bfloat16).astype(jnp.float32)
    gate_out = gate_total.astype(jnp.bfloat16).reshape(FF, N_COL, D // N_COL)
    up_out = up_total.astype(jnp.bfloat16).reshape(FF, N_COL, D // N_COL)
    return gate_out, up_out
```

```python
import jax
import jax.numpy as jnp
from jax import lax
from jax.sharding import Mesh, PartitionSpec as P

f32, bf16 = jnp.float32, jnp.bfloat16


def cotangents(gate_pre, up_value, grad_hidden):
    gate32 = gate_pre.astype(f32)
    sig = 1.0 / (1.0 + jnp.exp(-gate32))
    hid32 = grad_hidden.astype(f32)
    grad_up = (hid32 * gate32 * sig).astype(bf16)
    grad_gate = (hid32 * up_value.astype(f32) * sig * (1.0 + gate32 * (1.0 - sig))).astype(bf16)
    return grad_gate, grad_up


def refine(mesh):
    n_dp, n_row, n_col = mesh.devices.shape
    devs = mesh.devices.reshape(2, n_dp // 2, n_row // 2, 2, n_col)
    return Mesh(devs, ("a", "b", "z", "k", "l"))


def wrap(per_device, mesh):
    m = refine(mesh)
    in_specs = (
        P(("a", "b", "z", "k"), "l"),
        P(("a", "b", "l"), ("z", "k")),
        P(("a", "b", "l"), ("z", "k")),
        P(("a", "b", "l"), ("z", "k")),
    )
    out_specs = (P(("z", "k"), "l", ("a", "b")), P(("z", "k"), "l", ("a", "b")))
    return jax.shard_map(per_device, mesh=m, in_specs=in_specs, out_specs=out_specs, check_vma=False)

def per_device(x, gp, uv, gh):
    gg, gu = cotangents(gp, uv, gh)
    g = lax.all_gather(jnp.stack([gg, gu]), "l", axis=1, tiled=True)
    xs = lax.all_gather(x, ("z", "k"), axis=0, tiled=True)
    part = lax.dot_general(g, xs, (((1,), (0,)), ((), ())), preferred_element_type=f32)
    h, w = part.shape[1], part.shape[2]
    t = part.astype(bf16).reshape(2, h, 2, 4, w // 8).transpose(3, 2, 0, 1, 4)
    s1 = lax.psum_scatter(t, "b", scatter_dimension=0, tiled=True)[0]
    a = lax.axis_index("a")
    mine = lax.dynamic_index_in_dim(s1, a, axis=0, keepdims=False)
    other = lax.dynamic_index_in_dim(s1, 1 - a, axis=0, keepdims=False)
    got = lax.ppermute(other, "a", perm=[(0, 1), (1, 0)])
    s2 = (mine.astype(f32) + got.astype(f32)).astype(bf16)
    return s2[0].reshape(h, 1, -1), s2[1].reshape(h, 1, -1)

def solution(mesh):
    return wrap(per_device, mesh)
```

```python
import jax
import jax.numpy as jnp
from jax import lax
from jax.sharding import Mesh, PartitionSpec as P

f32, bf16 = jnp.float32, jnp.bfloat16


def cotangents(gate_pre, up_value, grad_hidden):
    gate32 = gate_pre.astype(f32)
    sig = 1.0 / (1.0 + jnp.exp(-gate32))
    hid32 = grad_hidden.astype(f32)
    grad_up = (hid32 * gate32 * sig).astype(bf16)
    grad_gate = (hid32 * up_value.astype(f32) * sig * (1.0 + gate32 * (1.0 - sig))).astype(bf16)
    return grad_gate, grad_up


def refine(mesh):
    n_dp, n_row, n_col = mesh.devices.shape
    devs = mesh.devices.reshape(2, n_dp // 2, n_row // 2, 2, n_col)
    return Mesh(devs, ("a", "b", "z", "k", "l"))


def wrap(per_device, mesh):
    m = refine(mesh)
    in_specs = (
        P(("a", "b", "z", "k"), "l"),
        P(("a", "b", "l"), ("z", "k")),
        P(("a", "b", "l"), ("z", "k")),
        P(("a", "b", "l"), ("z", "k")),
    )
    out_specs = (P(("z", "k"), "l", ("a", "b")), P(("z", "k"), "l", ("a", "b")))
    return jax.shard_map(per_device, mesh=m, in_specs=in_specs, out_specs=out_specs, check_vma=False)

def ring_z(x, nz):
    z = lax.axis_index("z")
    k = lax.axis_index("k")
    up = [(i, (i + 1) % nz) for i in range(nz)]
    dn = [(i, (i - 1) % nz) for i in range(nz)]
    kk = [(0, 1), (1, 0)]
    buf = jnp.zeros((nz, 2) + x.shape, x.dtype)
    def put(buf, blk, zz, kq):
        return lax.dynamic_update_slice(buf, blk[None, None], (zz, kq, 0, 0))
    buf = put(buf, x, z, k)
    buf = put(buf, lax.ppermute(x, "k", kk), z, 1 - k)
    f, b = x, x
    for s in range(1, nz // 2 + 1):
        f = lax.ppermute(f, "z", up)
        zz = (z - s) % nz
        buf = put(buf, f, zz, k)
        buf = put(buf, lax.ppermute(f, "k", kk), zz, 1 - k)
        if s < nz - s:
            b = lax.ppermute(b, "z", dn)
            zz = (z + s) % nz
            buf = put(buf, b, zz, k)
            buf = put(buf, lax.ppermute(b, "k", kk), zz, 1 - k)
    return buf


def per_device(x, gp, uv, gh):
    gg, gu = cotangents(gp, uv, gh)
    g, x = lax.optimization_barrier((jnp.stack([gg, gu]), x))
    g = lax.all_gather(g, "l", axis=1, tiled=True)
    xf = ring_z(x, lax.axis_size("z"))
    return finish(g, xf)

def reduce_out(part, a):
    h, w = part.shape
    tt = part.astype(bf16).reshape(h, 2, 4, w // 8).transpose(2, 1, 0, 3)
    s1 = lax.psum_scatter(tt, "b", scatter_dimension=0, tiled=True)[0]
    mine = lax.dynamic_index_in_dim(s1, a, axis=0, keepdims=False)
    other = lax.dynamic_index_in_dim(s1, 1 - a, axis=0, keepdims=False)
    got = lax.ppermute(other, "a", [(0, 1), (1, 0)])
    return (mine.astype(f32) + got.astype(f32)).astype(bf16).reshape(h, 1, -1)


def finish(g, xf):
    a = lax.axis_index("a")
    n_s, t, h = g.shape
    xf = xf.reshape(t, -1)
    dims = (((0,), (0,)), ((), ()))
    outs = []
    for s in range(n_s):
        part = lax.dot_general(g[s], xf, dims, preferred_element_type=f32)
        outs.append(reduce_out(part, a))
    return outs[0], outs[1]

def solution(mesh):
    return wrap(per_device, mesh)
```

```python
import jax
import jax.numpy as jnp
from jax import lax
from jax.sharding import Mesh, PartitionSpec as P

f32, bf16 = jnp.float32, jnp.bfloat16


def cotangents(gate_pre, up_value, grad_hidden):
    gate32 = gate_pre.astype(f32)
    sig = 1.0 / (1.0 + jnp.exp(-gate32))
    hid32 = grad_hidden.astype(f32)
    grad_up = (hid32 * gate32 * sig).astype(bf16)
    grad_gate = (hid32 * up_value.astype(f32) * sig * (1.0 + gate32 * (1.0 - sig))).astype(bf16)
    return grad_gate, grad_up


def refine(mesh):
    n_dp, n_row, n_col = mesh.devices.shape
    devs = mesh.devices.reshape(2, n_dp // 2, n_row // 2, 2, n_col)
    return Mesh(devs, ("a", "b", "z", "k", "l"))


def wrap(per_device, mesh):
    m = refine(mesh)
    in_specs = (
        P(("a", "b", "z", "k"), "l"),
        P(("a", "b", "l"), ("z", "k")),
        P(("a", "b", "l"), ("z", "k")),
        P(("a", "b", "l"), ("z", "k")),
    )
    out_specs = (P(("z", "k"), "l", ("a", "b")), P(("z", "k"), "l", ("a", "b")))
    return jax.shard_map(per_device, mesh=m, in_specs=in_specs, out_specs=out_specs, check_vma=False)

def ring_z(x, nz):
    z = lax.axis_index("z")
    k = lax.axis_index("k")
    up = [(i, (i + 1) % nz) for i in range(nz)]
    dn = [(i, (i - 1) % nz) for i in range(nz)]
    kk = [(0, 1), (1, 0)]
    buf = jnp.zeros((nz, 2) + x.shape, x.dtype)
    def put(buf, blk, zz, kq):
        return lax.dynamic_update_slice(buf, blk[None, None], (zz, kq, 0, 0))
    buf = put(buf, x, z, k)
    buf = put(buf, lax.ppermute(x, "k", kk), z, 1 - k)
    f, b = x, x
    for s in range(1, nz // 2 + 1):
        f = lax.ppermute(f, "z", up)
        zz = (z - s) % nz
        buf = put(buf, f, zz, k)
        buf = put(buf, lax.ppermute(f, "k", kk), zz, 1 - k)
        if s < nz - s:
            b = lax.ppermute(b, "z", dn)
            zz = (z + s) % nz
            buf = put(buf, b, zz, k)
            buf = put(buf, lax.ppermute(b, "k", kk), zz, 1 - k)
    return buf


def per_device(x, gp, uv, gh):
    gg, gu = cotangents(gp, uv, gh)
    g, x = lax.optimization_barrier((jnp.stack([gg, gu]), x))
    g = lax.all_gather(g, "l", axis=1, tiled=True)
    xf = ring_z(x, lax.axis_size("z"))
    return finish(g, xf)


def ring_rs(part, nb):
    b = lax.axis_index("b")
    h, w = part.shape
    c = w // (2 * nb)
    cw = [(i, (i + 1) % nb) for i in range(nb)]
    ccw = [(i, (i - 1) % nb) for i in range(nb)]
    def own(j, half):
        return lax.dynamic_slice_in_dim(part, half * (w // 2) + j * c, c, axis=1)
    m0 = own((b - 1) % nb, 0).astype(bf16)
    m1 = own((b + 1) % nb, 1).astype(bf16)
    for s in range(2, nb):
        m0 = (lax.ppermute(m0, "b", cw).astype(f32) + own((b - s) % nb, 0)).astype(bf16)
        m1 = (lax.ppermute(m1, "b", ccw).astype(f32) + own((b + s) % nb, 1)).astype(bf16)
    r0 = lax.ppermute(m0, "b", cw).astype(f32) + own(b, 0)
    r1 = lax.ppermute(m1, "b", ccw).astype(f32) + own(b, 1)
    return r0, r1


def one_out(gs, xf, a):
    part = lax.dot_general(gs, xf, (((0,), (0,)), ((), ())), preferred_element_type=f32)
    h = part.shape[0]
    r0, r1 = ring_rs(part, lax.axis_size("b"))
    mine = jnp.where(a == 0, r0, r1)
    other = jnp.where(a == 0, r1, r0).astype(bf16)
    got = lax.ppermute(other, "a", [(0, 1), (1, 0)])
    return (mine + got.astype(f32)).astype(bf16).reshape(h, 1, -1)


def finish(g, xf):
    a = lax.axis_index("a")
    n_s, t, h = g.shape
    xf = xf.reshape(t, -1)
    return one_out(g[0], xf, a), one_out(g[1], xf, a)

def solution(mesh):
    return wrap(per_device, mesh)
```

```python
import jax
import jax.numpy as jnp
from jax import lax
from jax.sharding import Mesh, PartitionSpec as P

f32, bf16 = jnp.float32, jnp.bfloat16


def cotangents(gate_pre, up_value, grad_hidden):
    gate32 = gate_pre.astype(f32)
    sig = 1.0 / (1.0 + jnp.exp(-gate32))
    hid32 = grad_hidden.astype(f32)
    grad_up = (hid32 * gate32 * sig).astype(bf16)
    grad_gate = (hid32 * up_value.astype(f32) * sig * (1.0 + gate32 * (1.0 - sig))).astype(bf16)
    return grad_gate, grad_up


def refine(mesh):
    n_dp, n_row, n_col = mesh.devices.shape
    devs = mesh.devices.reshape(2, n_dp // 2, n_row // 2, 2, n_col)
    return Mesh(devs, ("a", "b", "z", "k", "l"))


def wrap(per_device, mesh):
    m = refine(mesh)
    in_specs = (
        P(("a", "b", "z", "k"), "l"),
        P(("a", "b", "l"), ("z", "k")),
        P(("a", "b", "l"), ("z", "k")),
        P(("a", "b", "l"), ("z", "k")),
    )
    out_specs = (P(("z", "k"), "l", ("a", "b")), P(("z", "k"), "l", ("a", "b")))
    return jax.shard_map(per_device, mesh=m, in_specs=in_specs, out_specs=out_specs, check_vma=False)

def ring_z(x, nz):
    z = lax.axis_index("z")
    k = lax.axis_index("k")
    up = [(i, (i + 1) % nz) for i in range(nz)]
    dn = [(i, (i - 1) % nz) for i in range(nz)]
    kk = [(0, 1), (1, 0)]
    buf = jnp.zeros((nz, 2) + x.shape, x.dtype)
    def put(buf, blk, zz, kq):
        return lax.dynamic_update_slice(buf, blk[None, None], (zz, kq, 0, 0))
    buf = put(buf, x, z, k)
    buf = put(buf, lax.ppermute(x, "k", kk), z, 1 - k)
    f, b = x, x
    for s in range(1, nz // 2 + 1):
        f = lax.ppermute(f, "z", up)
        zz = (z - s) % nz
        buf = put(buf, f, zz, k)
        buf = put(buf, lax.ppermute(f, "k", kk), zz, 1 - k)
        if s < nz - s:
            b = lax.ppermute(b, "z", dn)
            zz = (z + s) % nz
            buf = put(buf, b, zz, k)
            buf = put(buf, lax.ppermute(b, "k", kk), zz, 1 - k)
    return buf


def per_device(x, gp, uv, gh):
    gg, gu = cotangents(gp, uv, gh)
    g, x = lax.optimization_barrier((jnp.stack([gg, gu]), x))
    nl = lax.axis_size("l")
    gb = jnp.broadcast_to(g[:, None], (g.shape[0], nl) + g.shape[1:])
    g = lax.all_to_all(gb, "l", 1, 1, tiled=True).reshape(g.shape[0], -1, g.shape[2])
    xf = ring_z(x, lax.axis_size("z"))
    return finish(g, xf)

def ring_rs(part, nb):
    b = lax.axis_index("b")
    h, w = part.shape
    c = w // (2 * nb)
    cw = [(i, (i + 1) % nb) for i in range(nb)]
    ccw = [(i, (i - 1) % nb) for i in range(nb)]
    def own(j, half):
        return lax.dynamic_slice_in_dim(part, half * (w // 2) + j * c, c, axis=1)
    m0 = own((b - 1) % nb, 0).astype(bf16)
    m1 = own((b + 1) % nb, 1).astype(bf16)
    for s in range(2, nb):
        m0 = (lax.ppermute(m0, "b", cw).astype(f32) + own((b - s) % nb, 0)).astype(bf16)
        m1 = (lax.ppermute(m1, "b", ccw).astype(f32) + own((b + s) % nb, 1)).astype(bf16)
    r0 = lax.ppermute(m0, "b", cw).astype(f32) + own(b, 0)
    r1 = lax.ppermute(m1, "b", ccw).astype(f32) + own(b, 1)
    return r0, r1


def one_out(gs, xf, a):
    part = lax.dot_general(gs, xf, (((0,), (0,)), ((), ())), preferred_element_type=f32)
    h = part.shape[0]
    r0, r1 = ring_rs(part, lax.axis_size("b"))
    mine = jnp.where(a == 0, r0, r1)
    other = jnp.where(a == 0, r1, r0).astype(bf16)
    got = lax.ppermute(other, "a", [(0, 1), (1, 0)])
    return (mine + got.astype(f32)).astype(bf16).reshape(h, 1, -1)


def finish(g, xf):
    a = lax.axis_index("a")
    n_s, t, h = g.shape
    xf = xf.reshape(t, -1)
    return one_out(g[0], xf, a), one_out(g[1], xf, a)

def solution(mesh):
    return wrap(per_device, mesh)
```
